512 devices in a mesh: context: 128 (over z, y, core), tensor: 4 (over x).
Axes of the slice: x: 4, y: 4, z: 16, core: 2. Of those that a mesh axis runs over, the one named last changes fastest.
Arguments:
- projected: bfloat16 [3, 16, 512, 16384], P(None, 'tensor', None, 'context'), may hold values from -6 to 6
- long_filter: bfloat16 [512, 128], replicated, may hold values from -0.5 to 0.5
- cotangent: bfloat16 [16, 512, 16384], P('tensor', None, 'context'), may hold values from -6 to 6
Outputs:
- mixed: bfloat16 [16, 512, 16384], P('tensor', None, 'context')
- stream_grads: bfloat16 [3, 16, 512, 16384], P(None, 'tensor', None, 'context')
- filter_grads: float32 [512, 128], P('context')
The draws below stay inside these ranges and needn't reach their ends.
All inputs are finite; a program needn't handle non-finite values.
Results may differ from the reference program's by a relative error of at most 0.0057.
Values may be sent and summed in bfloat16 or wider, within the bound.
No kernel may reach another device: no remote copies, remote signals or barrier semaphores. Data moves between devices by JAX's collectives and lax.ppermute only.
A program may use at most 64 MiB of HBM per device.

```python
import math
import jax
import jax.numpy as jnp
from jax import lax

GROUP = 16
TAPS = 128
NGROUPS = 512
LENGTH = 16384


def block_levels(stream_key, shape, shards, least, largest):
    loudness = 1.0
    for axis_at, shards_of in shards:
        heights = jax.random.uniform(jax.random.fold_in(jax.random.fold_in(stream_key, 6), axis_at), (shards_of,), jnp.float32, least / len(shards), largest / len(shards))
        loudness = loudness * jnp.repeat(jnp.exp(heights), shape[axis_at] // shards_of).reshape((-1,) + (1,) * (len(shape) - 1 - axis_at))
    return loudness


def noise(rng, dims, deviation, reach, shards=(), kind=jnp.bfloat16):
    factor_of = block_levels(rng, dims, shards, -0.22, 0.18) if shards else 1.0
    array = jax.random.normal(rng, dims, jnp.float32) * deviation * factor_of
    return jnp.minimum(jnp.maximum(array, -reach), reach).astype(kind)


def setup_inputs(seed: int = 0) -> dict:
    streams_of = jax.random.split(jax.random.key(seed), 4)
    return {
        "projected": noise(streams_of[0], (3, GROUP, NGROUPS, LENGTH), 1.0, 6.0, ((1, 4), (3, 128))),
        "long_filter": noise(streams_of[1], (NGROUPS, TAPS), TAPS ** -0.5, 0.5),
        "cotangent": noise(streams_of[2], (GROUP, NGROUPS, LENGTH), 1.0, 6.0, ((0, 4), (2, 128))),
    }


def toeplitz(filters):
    width, filter_taps = filters.shape
    padding = jnp.zeros((width, filter_taps), filters.dtype)
    flipped = jnp.concatenate([padding, filters[:, ::-1], padding], 1)
    stacked = jnp.broadcast_to(flipped[:, None, :], (width, filter_taps, 3 * filter_taps))
    stacked = stacked.reshape(width, 3 * filter_taps * filter_taps)
    stacked = jnp.concatenate([stacked, padding], 1)
    stacked = stacked.reshape(width, filter_taps, 3 * filter_taps + 1)[:, :, :2 * filter_taps]
    return stacked[:, ::-1]

def diagonal_sums(outer_sums):
    width, filter_taps, doubled = outer_sums.shape
    flattened = outer_sums.reshape(width, doubled * filter_taps)
    flattened = jnp.concatenate([flattened, jnp.zeros((width, filter_taps), outer_sums.dtype)], 1)
    flattened = flattened.reshape(width, filter_taps, doubled + 1)
    return lax.optimization_barrier(jnp.sum(flattened[:, :, 1:filter_taps + 1], 1))[:, ::-1]

def forward_block(paired, filters):
    matrices = toeplitz(filters).astype(jnp.float32)
    product = jnp.einsum('mgbk,gik->mgbi', paired.astype(jnp.float32), matrices)
    return product.astype(jnp.bfloat16)

def backward_block(grad_tiles, paired, filters):
    filter_taps = filters.shape[1]
    matrices = toeplitz(filters).astype(jnp.float32)
    grads_wide = grad_tiles.astype(jnp.float32)
    spread = jnp.einsum('mgbi,gik->mgbk', grads_wide, matrices)
    carried = jnp.concatenate([spread[:, :, 1:, :filter_taps], jnp.zeros_like(spread[:, :, :1, :filter_taps])], 2)
    grad_gated = (spread[:, :, :, filter_taps:] + carried).astype(jnp.bfloat16)
    outer_sums = jnp.einsum('mgbi,mgbk->gik', grads_wide, paired.astype(jnp.float32))
    return (grad_gated, diagonal_sums(outer_sums))

def group_blocks(tiles, block_count, width):
    members, groups, tile_count, extent = tiles.shape
    return tiles.reshape(members, block_count, width, tile_count, extent).transpose(1, 0, 2, 3, 4)

def join_blocks(blocked):
    block_count, members, width, tile_count, extent = blocked.shape
    return blocked.transpose(1, 0, 2, 3, 4).reshape(members, block_count * width, tile_count * extent)

def reference(projected, long_filter, cotangent):
    filter_taps = long_filter.shape[1]
    query_stream = projected[0].astype(jnp.float32)
    key_stream = projected[1].astype(jnp.float32)
    value_stream = projected[2].astype(jnp.float32)
    gated = (key_stream * value_stream).astype(jnp.bfloat16)
    members, groups, length = gated.shape
    tile_count = length // filter_taps
    tiles = gated.reshape(members, groups, tile_count, filter_taps)
    earlier = jnp.concatenate([jnp.zeros((members, groups, 1, filter_taps), jnp.bfloat16), tiles[:, :, :-1]], 2)
    paired = jnp.concatenate([earlier, tiles], 3)
    width = math.gcd(groups, 32)
    block_count = groups // width
    paired_blocks = group_blocks(paired, block_count, width)
    filter_blocks = long_filter.reshape(block_count, width, filter_taps)
    filtered = join_blocks(lax.map(lambda items: forward_block(items[0], items[1]), (paired_blocks, filter_blocks)))
    filtered_wide = filtered.astype(jnp.float32)
    mixed = (query_stream * filtered_wide).astype(jnp.bfloat16)
    cotangent_wide = cotangent.astype(jnp.float32)
    grad_filtered = (cotangent_wide * query_stream).astype(jnp.bfloat16)
    grad_blocks = group_blocks(grad_filtered.reshape(members, groups, tile_count, filter_taps), block_count, width)
    grad_pieces, sum_pieces = lax.map(lambda items: backward_block(items[0], items[1], items[2]), (grad_blocks, paired_blocks, filter_blocks))
    grad_gated = join_blocks(grad_pieces).astype(jnp.float32)
    filter_grads = sum_pieces.reshape(groups, filter_taps) / math.sqrt(members * length)
    stream_grads = jnp.stack([cotangent_wide * filtered_wide, grad_gated * value_stream, grad_gated * key_stream]).astype(jnp.bfloat16)
    return (mixed, stream_grads, filter_grads)
```

```python
import math

import jax
import jax.numpy as jnp
from jax import lax
from jax.sharding import PartitionSpec as P


def grouped_conv(lhs, rhs, groups):
    return lax.conv_general_dilated(
        lhs,
        rhs,
        window_strides=(1,),
        padding="VALID",
        dimension_numbers=("NCH", "OIH", "NCH"),
        feature_group_count=groups,
        preferred_element_type=jnp.float32,
    )


def body(projected, long_filter, cotangent):
    filter_taps = long_filter.shape[1]
    query_stream = projected[0]
    key_stream = projected[1]
    value_stream = projected[2]
    members, groups, local_tokens = key_stream.shape
    blocks = lax.axis_size("context")
    length = local_tokens * blocks
    factor = 1.0 / math.sqrt(members * lax.axis_size("tensor") * length)
    gated = (key_stream.astype(jnp.float32) * value_stream.astype(jnp.float32)).astype(jnp.bfloat16)
    grad_filtered = (cotangent.astype(jnp.float32) * query_stream.astype(jnp.float32)).astype(
        jnp.bfloat16
    )
    earlier = lax.ppermute(gated, "context", [(i, i + 1) for i in range(blocks - 1)])
    later = lax.ppermute(grad_filtered, "context", [(i + 1, i) for i in range(blocks - 1)])
    halo = filter_taps - 1
    gated_ext = jnp.concatenate([earlier[:, :, local_tokens - halo:], gated], 2)
    grad_ext = jnp.concatenate([grad_filtered, later[:, :, :halo]], 2)
    reversed_taps = long_filter[:, ::-1][:, None, :]
    filtered = grouped_conv(gated_ext, reversed_taps, groups).astype(jnp.bfloat16)
    grad_gated = grouped_conv(grad_ext, long_filter[:, None, :], groups).astype(jnp.bfloat16)
    tap_sums = lax.conv_general_dilated(
        gated_ext,
        grad_filtered,
        window_strides=(1,),
        padding=((0, 0),),
        dimension_numbers=lax.ConvDimensionNumbers((1, 0, 2), (1, 0, 2), (1, 0, 2)),
        batch_group_count=groups,
        preferred_element_type=jnp.float32,
    )
    partial_taps = tap_sums[:, 0, ::-1]
    own_taps = lax.psum_scatter(partial_taps, "context", scatter_dimension=0, tiled=True)
    filter_grads = lax.psum(own_taps, "tensor") * factor
    filtered_wide = filtered.astype(jnp.float32)
    grad_wide = grad_gated.astype(jnp.float32)
    mixed = (query_stream.astype(jnp.float32) * filtered_wide).astype(jnp.bfloat16)
    stream_grads = jnp.stack(
        [
            cotangent.astype(jnp.float32) * filtered_wide,
            grad_wide * value_stream.astype(jnp.float32),
            grad_wide * key_stream.astype(jnp.float32),
        ]
    ).astype(jnp.bfloat16)
    return (mixed, stream_grads, filter_grads)


def solution(mesh):
    in_specs = (P(None, "tensor", None, "context"), P(), P("tensor", None, "context"))
    out_specs = (
        P("tensor", None, "context"),
        P(None, "tensor", None, "context"),
        P("context", None),
    )
    return jax.shard_map(body, mesh=mesh, in_specs=in_specs, out_specs=out_specs, check_vma=False)
```

```python
import math

import jax
import jax.numpy as jnp
from jax import lax
from jax.sharding import PartitionSpec as P


def grouped_conv(lhs, rhs, groups):
    return lax.conv_general_dilated(
        lhs,
        rhs,
        window_strides=(1,),
        padding="VALID",
        dimension_numbers=("NCH", "OIH", "NCH"),
        feature_group_count=groups,
        preferred_element_type=jnp.float32,
    )


def halving_sum(rows, axis):
    size = lax.axis_size(axis)
    index = lax.axis_index(axis)
    bit = 0
    while (1 << bit) < size:
        split = rows.reshape((rows.shape[0] // 2, 2) + rows.shape[1:])
        upper = ((index >> bit) & 1) == 1
        keep = jnp.where(upper, split[:, 1], split[:, 0])
        give = jnp.where(upper, split[:, 0], split[:, 1])
        pairs = [(i, i ^ (1 << bit)) for i in range(size)]
        rows = keep + lax.ppermute(give, axis, pairs)
        bit += 1
    return rows


def butterfly_sum(values, axis):
    size = lax.axis_size(axis)
    bit = 0
    while (1 << bit) < size:
        pairs = [(i, i ^ (1 << bit)) for i in range(size)]
        values = values + lax.ppermute(values, axis, pairs)
        bit += 1
    return values


def body(projected, long_filter, cotangent):
    filter_taps = long_filter.shape[1]
    query_stream = projected[0]
    key_stream = projected[1]
    value_stream = projected[2]
    members, groups, local_tokens = key_stream.shape
    blocks = lax.axis_size("context")
    length = local_tokens * blocks
    factor = 1.0 / math.sqrt(members * lax.axis_size("tensor") * length)
    gated = (key_stream.astype(jnp.float32) * value_stream.astype(jnp.float32)).astype(jnp.bfloat16)
    grad_filtered = (cotangent.astype(jnp.float32) * query_stream.astype(jnp.float32)).astype(
        jnp.bfloat16
    )
    earlier = lax.ppermute(gated, "context", [(i, i + 1) for i in range(blocks - 1)])
    later = lax.ppermute(grad_filtered, "context", [(i + 1, i) for i in range(blocks - 1)])
    halo = filter_taps - 1
    gated_ext = jnp.concatenate([earlier[:, :, local_tokens - halo:], gated], 2)
    grad_ext = jnp.concatenate([grad_filtered, later[:, :, :halo]], 2)
    reversed_taps = long_filter[:, ::-1][:, None, :]
    filtered = grouped_conv(gated_ext, reversed_taps, groups).astype(jnp.bfloat16)
    grad_gated = grouped_conv(grad_ext, long_filter[:, None, :], groups).astype(jnp.bfloat16)
    tap_sums = lax.conv_general_dilated(
        gated_ext,
        grad_filtered,
        window_strides=(1,),
        padding=((0, 0),),
        dimension_numbers=lax.ConvDimensionNumbers((1, 0, 2), (1, 0, 2), (1, 0, 2)),
        batch_group_count=groups,
        preferred_element_type=jnp.float32,
    )
    partial_taps = tap_sums[:, 0, ::-1]
    own_taps = halving_sum(partial_taps.reshape(blocks, groups // blocks, filter_taps), "context")
    filter_grads = butterfly_sum(own_taps[0], "tensor") * factor
    filtered_wide = filtered.astype(jnp.float32)
    grad_wide = grad_gated.astype(jnp.float32)
    mixed = (query_stream.astype(jnp.float32) * filtered_wide).astype(jnp.bfloat16)
    stream_grads = jnp.stack(
        [
            cotangent.astype(jnp.float32) * filtered_wide,
            grad_wide * value_stream.astype(jnp.float32),
            grad_wide * key_stream.astype(jnp.float32),
        ]
    ).astype(jnp.bfloat16)
    return (mixed, stream_grads, filter_grads)


def solution(mesh):
    in_specs = (P(None, "tensor", None, "context"), P(), P("tensor", None, "context"))
    out_specs = (
        P("tensor", None, "context"),
        P(None, "tensor", None, "context"),
        P("context", None),
    )
    return jax.shard_map(body, mesh=mesh, in_specs=in_specs, out_specs=out_specs, check_vma=False)
```

```python
import math

import jax
import jax.numpy as jnp
from jax import lax
from jax.sharding import PartitionSpec as P

CONTEXT = ("z", "y", "core")


def grouped_conv(lhs, rhs, groups):
    return lax.conv_general_dilated(
        lhs,
        rhs,
        window_strides=(1,),
        padding="VALID",
        dimension_numbers=("NCH", "OIH", "NCH"),
        feature_group_count=groups,
        preferred_element_type=jnp.float32,
    )


def halving_sum(rows, axis):
    size = lax.axis_size(axis)
    index = lax.axis_index(axis)
    bit = 0
    while (1 << bit) < size:
        split = rows.reshape((rows.shape[0] // 2, 2) + rows.shape[1:])
        upper = ((index >> bit) & 1) == 1
        keep = jnp.where(upper, split[:, 1], split[:, 0])
        give = jnp.where(upper, split[:, 0], split[:, 1])
        pairs = [(i, i ^ (1 << bit)) for i in range(size)]
        rows = keep + lax.ppermute(give, axis, pairs)
        bit += 1
    return rows


def butterfly_sum(values, axis):
    size = lax.axis_size(axis)
    bit = 0
    while (1 << bit) < size:
        pairs = [(i, i ^ (1 << bit)) for i in range(size)]
        values = values + lax.ppermute(values, axis, pairs)
        bit += 1
    return values


def body(projected, long_filter, cotangent):
    filter_taps = long_filter.shape[1]
    query_stream = projected[0]
    key_stream = projected[1]
    value_stream = projected[2]
    members, groups, local_tokens = key_stream.shape
    blocks = lax.axis_size(CONTEXT)
    length = local_tokens * blocks
    factor = 1.0 / math.sqrt(members * lax.axis_size("tensor") * length)
    gated = (key_stream.astype(jnp.float32) * value_stream.astype(jnp.float32)).astype(jnp.bfloat16)
    grad_filtered = (cotangent.astype(jnp.float32) * query_stream.astype(jnp.float32)).astype(
        jnp.bfloat16
    )
    earlier = lax.ppermute(gated, CONTEXT, [(i, i + 1) for i in range(blocks - 1)])
    later = lax.ppermute(grad_filtered, CONTEXT, [(i + 1, i) for i in range(blocks - 1)])
    halo = filter_taps - 1
    gated_ext = jnp.concatenate([earlier[:, :, local_tokens - halo:], gated], 2)
    grad_ext = jnp.concatenate([grad_filtered, later[:, :, :halo]], 2)
    reversed_taps = long_filter[:, ::-1][:, None, :]
    filtered = grouped_conv(gated_ext, reversed_taps, groups).astype(jnp.bfloat16)
    grad_gated = grouped_conv(grad_ext, long_filter[:, None, :], groups).astype(jnp.bfloat16)
    tap_sums = lax.conv_general_dilated(
        gated_ext,
        grad_filtered,
        window_strides=(1,),
        padding=((0, 0),),
        dimension_numbers=lax.ConvDimensionNumbers((1, 0, 2), (1, 0, 2), (1, 0, 2)),
        batch_group_count=groups,
        preferred_element_type=jnp.float32,
    )
    partial_taps = tap_sums[:, 0, ::-1]
    rows = partial_taps.reshape(blocks, groups // blocks, filter_taps)
    rows = halving_sum(halving_sum(rows, "core"), "y")
    rows = lax.all_to_all(rows, "z", split_axis=0, concat_axis=0, tiled=True)
    own_taps = jnp.sum(rows, axis=0, keepdims=True)
    filter_grads = butterfly_sum(own_taps[0], "tensor") * factor
    filtered_wide = filtered.astype(jnp.float32)
    grad_wide = grad_gated.astype(jnp.float32)
    mixed = (query_stream.astype(jnp.float32) * filtered_wide).astype(jnp.bfloat16)
    stream_grads = jnp.stack(
        [
            cotangent.astype(jnp.float32) * filtered_wide,
            grad_wide * value_stream.astype(jnp.float32),
            grad_wide * key_stream.astype(jnp.float32),
        ]
    ).astype(jnp.bfloat16)
    return (mixed, stream_grads, filter_grads)


def solution(mesh):
    contexts, tensors = mesh.devices.shape
    split = mesh.devices.reshape(contexts // 8, 4, 2, tensors)
    fine = jax.sharding.Mesh(split, CONTEXT + ("tensor",))
    in_specs = (P(None, "tensor", None, CONTEXT), P(), P("tensor", None, CONTEXT))
    out_specs = (
        P("tensor", None, CONTEXT),
        P(None, "tensor", None, CONTEXT),
        P(CONTEXT, None),
    )
    return jax.shard_map(body, mesh=fine, in_specs=in_specs, out_specs=out_specs, check_vma=False)
```

```python
import math

import jax
import jax.numpy as jnp
from jax import lax
from jax.sharding import PartitionSpec as P

CONTEXT = ("z", "y", "core")


def grouped_conv(lhs, rhs, groups):
    return lax.conv_general_dilated(
        lhs,
        rhs,
        window_strides=(1,),
        padding="VALID",
        dimension_numbers=("NCH", "OIH", "NCH"),
        feature_group_count=groups,
        preferred_element_type=jnp.float32,
    )


def halving_step(rows, axis, bit, cover=None):
    size = lax.axis_size(axis)
    index = lax.axis_index(axis)
    split = rows.reshape((rows.shape[0] // 2, 2) + rows.shape[1:])
    upper = ((index >> bit) & 1) == 1
    keep = jnp.where(upper, split[:, 1], split[:, 0])
    give = jnp.where(upper, split[:, 0], split[:, 1])
    pairs = [(i, i ^ (1 << bit)) for i in range(size)]
    if cover is None:
        return keep + lax.ppermute(give, axis, pairs)
    work, operands = cover
    give, operands = lax.optimization_barrier((give, operands))
    received = lax.ppermute(give, axis, pairs)
    received, done = lax.optimization_barrier((received, work(*operands)))
    return (keep + received, done)


def butterfly_sum(values, axis):
    size = lax.axis_size(axis)
    bit = 0
    while (1 << bit) < size:
        pairs = [(i, i ^ (1 << bit)) for i in range(size)]
        values = values + lax.ppermute(values, axis, pairs)
        bit += 1
    return values


def body(projected, long_filter, cotangent):
    filter_taps = long_filter.shape[1]
    query_stream = projected[0]
    key_stream = projected[1]
    value_stream = projected[2]
    members, groups, local_tokens = key_stream.shape
    blocks = lax.axis_size(CONTEXT)
    length = local_tokens * blocks
    factor = 1.0 / math.sqrt(members * lax.axis_size("tensor") * length)
    gated = (key_stream.astype(jnp.float32) * value_stream.astype(jnp.float32)).astype(jnp.bfloat16)
    grad_filtered = (cotangent.astype(jnp.float32) * query_stream.astype(jnp.float32)).astype(
        jnp.bfloat16
    )
    earlier = lax.ppermute(gated, CONTEXT, [(i, i + 1) for i in range(blocks - 1)])
    later = lax.ppermute(grad_filtered, CONTEXT, [(i + 1, i) for i in range(blocks - 1)])
    halo = filter_taps - 1
    gated_ext = jnp.concatenate([earlier[:, :, local_tokens - halo:], gated], 2)
    grad_ext = jnp.concatenate([grad_filtered, later[:, :, :halo]], 2)
    reversed_taps = long_filter[:, ::-1][:, None, :]
    tap_sums = lax.conv_general_dilated(
        gated_ext,
        grad_filtered,
        window_strides=(1,),
        padding=((0, 0),),
        dimension_numbers=lax.ConvDimensionNumbers((1, 0, 2), (1, 0, 2), (1, 0, 2)),
        batch_group_count=groups,
        preferred_element_type=jnp.float32,
    )
    partial_taps = tap_sums[:, 0, ::-1]
    rows = partial_taps.reshape(blocks, groups // blocks, filter_taps)
    forward = lambda lhs, rhs: grouped_conv(lhs, rhs, groups).astype(jnp.bfloat16)
    rows = halving_step(rows, "core", 0)
    rows, filtered = halving_step(rows, "y", 0, (forward, (gated_ext, reversed_taps)))
    rows, grad_gated = halving_step(rows, "y", 1, (forward, (grad_ext, long_filter[:, None, :])))
    rows = lax.all_to_all(rows, "z", split_axis=0, concat_axis=0, tiled=True)
    own_taps = jnp.sum(rows, axis=0, keepdims=True)
    filter_grads = butterfly_sum(own_taps[0], "tensor") * factor
    filtered_wide = filtered.astype(jnp.float32)
    grad_wide = grad_gated.astype(jnp.float32)
    mixed = (query_stream.astype(jnp.float32) * filtered_wide).astype(jnp.bfloat16)
    stream_grads = jnp.stack(
        [
            cotangent.astype(jnp.float32) * filtered_wide,
            grad_wide * value_stream.astype(jnp.float32),
            grad_wide * key_stream.astype(jnp.float32),
        ]
    ).astype(jnp.bfloat16)
    return (mixed, stream_grads, filter_grads)


def solution(mesh):
    contexts, tensors = mesh.devices.shape
    split = mesh.devices.reshape(contexts // 8, 4, 2, tensors)
    fine = jax.sharding.Mesh(split, CONTEXT + ("tensor",))
    in_specs = (P(None, "tensor", None, CONTEXT), P(), P("tensor", None, CONTEXT))
    out_specs = (
        P("tensor", None, CONTEXT),
        P(None, "tensor", None, CONTEXT),
        P(CONTEXT, None),
    )
    return jax.shard_map(body, mesh=fine, in_specs=in_specs, out_specs=out_specs, check_vma=False)
```

```python
import math

import jax
import jax.numpy as jnp
from jax import lax
from jax.sharding import PartitionSpec as P

CONTEXT = ("z", "y", "core")


def grouped_conv(lhs, rhs, groups):
    return lax.conv_general_dilated(
        lhs,
        rhs,
        window_strides=(1,),
        padding="VALID",
        dimension_numbers=("NCH", "OIH", "NCH"),
        feature_group_count=groups,
        preferred_element_type=jnp.float32,
    )


def halving_step(rows, axis, bit, cover=None):
    size = lax.axis_size(axis)
    index = lax.axis_index(axis)
    split = rows.reshape((rows.shape[0] // 2, 2) + rows.shape[1:])
    upper = ((index >> bit) & 1) == 1
    keep = jnp.where(upper, split[:, 1], split[:, 0])
    give = jnp.where(upper, split[:, 0], split[:, 1])
    pairs = [(i, i ^ (1 << bit)) for i in range(size)]
    if cover is None:
        return keep + lax.ppermute(give, axis, pairs)
    work, operands = cover
    give, operands = lax.optimization_barrier((give, operands))
    received = lax.ppermute(give, axis, pairs)
    received, done = lax.optimization_barrier((received, work(*operands)))
    return (keep + received, done)


def butterfly_sum(values, axis):
    size = lax.axis_size(axis)
    bit = 0
    while (1 << bit) < size:
        pairs = [(i, i ^ (1 << bit)) for i in range(size)]
        values = values + lax.ppermute(values, axis, pairs)
        bit += 1
    return values


def body(projected, long_filter, cotangent):
    filter_taps = long_filter.shape[1]
    query_stream = projected[0]
    key_stream = projected[1]
    value_stream = projected[2]
    members, groups, local_tokens = key_stream.shape
    blocks = lax.axis_size(CONTEXT)
    length = local_tokens * blocks
    factor = 1.0 / math.sqrt(members * lax.axis_size("tensor") * length)
    gated = (key_stream.astype(jnp.float32) * value_stream.astype(jnp.float32)).astype(jnp.bfloat16)
    grad_filtered = (cotangent.astype(jnp.float32) * query_stream.astype(jnp.float32)).astype(
        jnp.bfloat16
    )
    earlier = lax.ppermute(gated, CONTEXT, [(i, i + 1) for i in range(blocks - 1)])
    later = lax.ppermute(grad_filtered, CONTEXT, [(i + 1, i) for i in range(blocks - 1)])
    halo = filter_taps - 1
    gated_ext = jnp.concatenate([earlier[:, :, local_tokens - halo:], gated], 2)
    grad_ext = jnp.concatenate([grad_filtered, later[:, :, :halo]], 2)
    reversed_taps = long_filter[:, ::-1][:, None, :]
    tap_sums = lax.conv_general_dilated(
        gated_ext,
        grad_filtered,
        window_strides=(1,),
        padding=((0, 0),),
        dimension_numbers=lax.ConvDimensionNumbers((1, 0, 2), (1, 0, 2), (1, 0, 2)),
        batch_group_count=groups,
        preferred_element_type=jnp.float32,
    )
    partial_taps = tap_sums[:, 0, ::-1]
    rows = partial_taps.reshape(blocks, groups // blocks, filter_taps)
    forward = lambda lhs, rhs: grouped_conv(lhs, rhs, groups).astype(jnp.bfloat16)
    rows = halving_step(rows, "core", 0)
    rows, filtered = halving_step(rows, "y", 0, (forward, (gated_ext, reversed_taps)))
    rows = halving_step(rows, "y", 1)
    rows, operands = lax.optimization_barrier((rows, (grad_ext, long_filter[:, None, :])))
    rows = lax.all_to_all(rows, "z", split_axis=0, concat_axis=0, tiled=True)
    rows, grad_gated = lax.optimization_barrier((rows, forward(*operands)))
    own_taps = jnp.sum(rows, axis=0, keepdims=True)
    filter_grads = butterfly_sum(own_taps[0], "tensor") * factor
    filtered_wide = filtered.astype(jnp.float32)
    grad_wide = grad_gated.astype(jnp.float32)
    mixed = (query_stream.astype(jnp.float32) * filtered_wide).astype(jnp.bfloat16)
    stream_grads = jnp.stack(
        [
            cotangent.astype(jnp.float32) * filtered_wide,
            grad_wide * value_stream.astype(jnp.float32),
            grad_wide * key_stream.astype(jnp.float32),
        ]
    ).astype(jnp.bfloat16)
    return (mixed, stream_grads, filter_grads)


def solution(mesh):
    contexts, tensors = mesh.devices.shape
    split = mesh.devices.reshape(contexts // 8, 4, 2, tensors)
    fine = jax.sharding.Mesh(split, CONTEXT + ("tensor",))
    in_specs = (P(None, "tensor", None, CONTEXT), P(), P("tensor", None, CONTEXT))
    out_specs = (
        P("tensor", None, CONTEXT),
        P(None, "tensor", None, CONTEXT),
        P(CONTEXT, None),
    )
    return jax.shard_map(body, mesh=fine, in_specs=in_specs, out_specs=out_specs, check_vma=False)
```

```python
import math

import jax
import jax.numpy as jnp
from jax import lax
from jax.sharding import PartitionSpec as P

CONTEXT = ("z", "y", "core")


def grouped_conv(lhs, rhs, groups):
    return lax.conv_general_dilated(
        lhs,
        rhs,
        window_strides=(1,),
        padding="VALID",
        dimension_numbers=("NCH", "OIH", "NCH"),
        feature_group_count=groups,
        preferred_element_type=jnp.float32,
    )


def halving_step(rows, axis, bit, cover=None):
    size = lax.axis_size(axis)
    index = lax.axis_index(axis)
    split = rows.reshape((rows.shape[0] // 2, 2) + rows.shape[1:])
    upper = ((index >> bit) & 1) == 1
    keep = jnp.where(upper, split[:, 1], split[:, 0])
    give = jnp.where(upper, split[:, 0], split[:, 1])
    pairs = [(i, i ^ (1 << bit)) for i in range(size)]
    if cover is None:
        return keep + lax.ppermute(give, axis, pairs)
    work, operands = cover
    give, operands = lax.optimization_barrier((give, operands))
    received = lax.ppermute(give, axis, pairs)
    received, done = lax.optimization_barrier((received, work(*operands)))
    return (keep + received, done)


def butterfly_sum(values, axis):
    size = lax.axis_size(axis)
    bit = 0
    while (1 << bit) < size:
        pairs = [(i, i ^ (1 << bit)) for i in range(size)]
        values = values + lax.ppermute(values, axis, pairs)
        bit += 1
    return values


def body(projected, long_filter, cotangent):
    filter_taps = long_filter.shape[1]
    query_stream = projected[0]
    key_stream = projected[1]
    value_stream = projected[2]
    members, groups, local_tokens = key_stream.shape
    blocks = lax.axis_size(CONTEXT)
    length = local_tokens * blocks
    factor = 1.0 / math.sqrt(members * lax.axis_size("tensor") * length)
    gated = (key_stream.astype(jnp.float32) * value_stream.astype(jnp.float32)).astype(jnp.bfloat16)
    grad_filtered = (cotangent.astype(jnp.float32) * query_stream.astype(jnp.float32)).astype(
        jnp.bfloat16
    )
    earlier = lax.ppermute(gated, CONTEXT, [(i, i + 1) for i in range(blocks - 1)])
    later = lax.ppermute(grad_filtered, CONTEXT, [(i + 1, i) for i in range(blocks - 1)])
    halo = filter_taps - 1
    gated_ext = jnp.concatenate([earlier[:, :, local_tokens - halo:], gated], 2)
    grad_ext = jnp.concatenate([grad_filtered, later[:, :, :halo]], 2)
    reversed_taps = long_filter[:, ::-1][:, None, :]
    tap_sums = lax.conv_general_dilated(
        gated_ext,
        grad_filtered,
        window_strides=(1,),
        padding=((0, 0),),
        dimension_numbers=lax.ConvDimensionNumbers((1, 0, 2), (1, 0, 2), (1, 0, 2)),
        batch_group_count=groups,
        preferred_element_type=jnp.float32,
    )
    partial_taps = tap_sums[:, 0, ::-1]
    rows = partial_taps.reshape(blocks, groups // blocks, filter_taps)
    forward = lambda lhs, rhs: grouped_conv(lhs, rhs, groups).astype(jnp.bfloat16)
    rows = halving_step(rows, "core", 0)
    rows, filtered = halving_step(rows, "y", 0, (forward, (gated_ext, reversed_taps)))
    rows = halving_step(rows, "y", 1)
    rows, operands = lax.optimization_barrier((rows, (grad_ext, long_filter[:, None, :])))
    tensors = lax.axis_size("tensor")
    rows = jnp.broadcast_to(rows[:, None], (rows.shape[0], tensors) + rows.shape[1:])
    rows = rows.reshape((-1,) + rows.shape[2:])
    rows = lax.all_to_all(rows, ("z", "tensor"), split_axis=0, concat_axis=0, tiled=True)
    rows, grad_gated = lax.optimization_barrier((rows, forward(*operands)))
    filter_grads = jnp.sum(rows, axis=0) * factor
    filtered_wide = filtered.astype(jnp.float32)
    grad_wide = grad_gated.astype(jnp.float32)
    mixed = (query_stream.astype(jnp.float32) * filtered_wide).astype(jnp.bfloat16)
    stream_grads = jnp.stack(
        [
            cotangent.astype(jnp.float32) * filtered_wide,
            grad_wide * value_stream.astype(jnp.float32),
            grad_wide * key_stream.astype(jnp.float32),
        ]
    ).astype(jnp.bfloat16)
    return (mixed, stream_grads, filter_grads)


def solution(mesh):
    contexts, tensors = mesh.devices.shape
    split = mesh.devices.reshape(contexts // 8, 4, 2, tensors)
    fine = jax.sharding.Mesh(split, CONTEXT + ("tensor",))
    in_specs = (P(None, "tensor", None, CONTEXT), P(), P("tensor", None, CONTEXT))
    out_specs = (
        P("tensor", None, CONTEXT),
        P(None, "tensor", None, CONTEXT),
        P(CONTEXT, None),
    )
    return jax.shard_map(body, mesh=fine, in_specs=in_specs, out_specs=out_specs, check_vma=False)
```

```python
import math

import jax
import jax.numpy as jnp
from jax import lax
from jax.sharding import PartitionSpec as P

CONTEXT = ("z", "y", "core")


def grouped_conv(lhs, rhs, groups):
    return lax.conv_general_dilated(
        lhs,
        rhs,
        window_strides=(1,),
        padding="VALID",
        dimension_numbers=("NCH", "OIH", "NCH"),
        feature_group_count=groups,
        preferred_element_type=jnp.float32,
    )


def halving_step(rows, axis, bit, cover=None):
    size = lax.axis_size(axis)
    index = lax.axis_index(axis)
    split = rows.reshape((rows.shape[0] // 2, 2) + rows.shape[1:])
    upper = ((index >> bit) & 1) == 1
    keep = jnp.where(upper, split[:, 1], split[:, 0])
    give = jnp.where(upper, split[:, 0], split[:, 1])
    pairs = [(i, i ^ (1 << bit)) for i in range(size)]
    if cover is None:
        return keep + lax.ppermute(give, axis, pairs)
    work, operands = cover
    give, operands = lax.optimization_barrier((give, operands))
    received = lax.ppermute(give, axis, pairs)
    received, done = lax.optimization_barrier((received, work(*operands)))
    return (keep + received, done)


def butterfly_sum(values, axis):
    size = lax.axis_size(axis)
    bit = 0
    while (1 << bit) < size:
        pairs = [(i, i ^ (1 << bit)) for i in range(size)]
        values = values + lax.ppermute(values, axis, pairs)
        bit += 1
    return values


def body(projected, long_filter, cotangent):
    filter_taps = long_filter.shape[1]
    query_stream = projected[0]
    key_stream = projected[1]
    value_stream = projected[2]
    members, groups, local_tokens = key_stream.shape
    blocks = lax.axis_size(CONTEXT)
    length = local_tokens * blocks
    factor = 1.0 / math.sqrt(members * lax.axis_size("tensor") * length)
    gated = (key_stream.astype(jnp.float32) * value_stream.astype(jnp.float32)).astype(jnp.bfloat16)
    grad_filtered = (cotangent.astype(jnp.float32) * query_stream.astype(jnp.float32)).astype(
        jnp.bfloat16
    )
    earlier = lax.ppermute(gated, CONTEXT, [(i, i + 1) for i in range(blocks - 1)])
    halo = filter_taps - 1
    gated_ext = jnp.concatenate([earlier[:, :, local_tokens - halo:], gated], 2)
    reversed_taps = long_filter[:, ::-1][:, None, :]
    tap_sums = lax.conv_general_dilated(
        gated_ext,
        grad_filtered,
        window_strides=(1,),
        padding=((0, 0),),
        dimension_numbers=lax.ConvDimensionNumbers((1, 0, 2), (1, 0, 2), (1, 0, 2)),
        batch_group_count=groups,
        preferred_element_type=jnp.float32,
    )
    partial_taps = tap_sums[:, 0, ::-1]
    sent, partial_taps = lax.optimization_barrier((grad_filtered, partial_taps))
    later = lax.ppermute(sent, CONTEXT, [(i + 1, i) for i in range(blocks - 1)])
    grad_ext = jnp.concatenate([grad_filtered, later[:, :, :halo]], 2)
    rows = partial_taps.reshape(blocks, groups // blocks, filter_taps)
    forward = lambda lhs, rhs: grouped_conv(lhs, rhs, groups).astype(jnp.bfloat16)
    rows = halving_step(rows, "core", 0)
    rows, filtered = halving_step(rows, "y", 0, (forward, (gated_ext, reversed_taps)))
    rows = halving_step(rows, "y", 1)
    rows, operands = lax.optimization_barrier((rows, (grad_ext, long_filter[:, None, :])))
    rows = lax.all_to_all(rows, "z", split_axis=0, concat_axis=0, tiled=True)
    rows, grad_gated = lax.optimization_barrier((rows, forward(*operands)))
    own_taps = jnp.sum(rows, axis=0, keepdims=True)
    filter_grads = butterfly_sum(own_taps[0], "tensor") * factor
    filtered_wide = filtered.astype(jnp.float32)
    grad_wide = grad_gated.astype(jnp.float32)
    mixed = (query_stream.astype(jnp.float32) * filtered_wide).astype(jnp.bfloat16)
    stream_grads = jnp.stack(
        [
            cotangent.astype(jnp.float32) * filtered_wide,
            grad_wide * value_stream.astype(jnp.float32),
            grad_wide * key_stream.astype(jnp.float32),
        ]
    ).astype(jnp.bfloat16)
    return (mixed, stream_grads, filter_grads)


def solution(mesh):
    contexts, tensors = mesh.devices.shape
    split = mesh.devices.reshape(contexts // 8, 4, 2, tensors)
    fine = jax.sharding.Mesh(split, CONTEXT + ("tensor",))
    in_specs = (P(None, "tensor", None, CONTEXT), P(), P("tensor", None, CONTEXT))
    out_specs = (
        P("tensor", None, CONTEXT),
        P(None, "tensor", None, CONTEXT),
        P(CONTEXT, None),
    )
    return jax.shard_map(body, mesh=fine, in_specs=in_specs, out_specs=out_specs, check_vma=False)
```

```python
import math

import jax
import jax.numpy as jnp
from jax import lax
from jax.sharding import PartitionSpec as P

CONTEXT = ("z", "y", "core")


def grouped_conv(lhs, rhs, groups):
    return lax.conv_general_dilated(
        lhs,
        rhs,
        window_strides=(1,),
        padding="VALID",
        dimension_numbers=("NCH", "OIH", "NCH"),
        feature_group_count=groups,
        preferred_element_type=jnp.float32,
    )


def halving_step(rows, axis, bit, cover=None):
    size = lax.axis_size(axis)
    index = lax.axis_index(axis)
    split = rows.reshape((rows.shape[0] // 2, 2) + rows.shape[1:])
    upper = ((index >> bit) & 1) == 1
    keep = jnp.where(upper, split[:, 1], split[:, 0])
    give = jnp.where(upper, split[:, 0], split[:, 1])
    pairs = [(i, i ^ (1 << bit)) for i in range(size)]
    if cover is None:
        return keep + lax.ppermute(give, axis, pairs)
    work, operands = cover
    give, operands = lax.optimization_barrier((give, operands))
    received = lax.ppermute(give, axis, pairs)
    received, done = lax.optimization_barrier((received, work(*operands)))
    return (keep + received, done)


def butterfly_sum(values, axis):
    size = lax.axis_size(axis)
    bit = 0
    while (1 << bit) < size:
        pairs = [(i, i ^ (1 << bit)) for i in range(size)]
        values = values + lax.ppermute(values, axis, pairs)
        bit += 1
    return values


def body(projected, long_filter, cotangent):
    filter_taps = long_filter.shape[1]
    query_stream = projected[0]
    key_stream = projected[1]
    value_stream = projected[2]
    members, groups, local_tokens = key_stream.shape
    blocks = lax.axis_size(CONTEXT)
    length = local_tokens * blocks
    factor = 1.0 / math.sqrt(members * lax.axis_size("tensor") * length)
    gated = (key_stream.astype(jnp.float32) * value_stream.astype(jnp.float32)).astype(jnp.bfloat16)
    grad_filtered = (cotangent.astype(jnp.float32) * query_stream.astype(jnp.float32)).astype(
        jnp.bfloat16
    )
    earlier = lax.ppermute(gated, CONTEXT, [(i, i + 1) for i in range(blocks - 1)])
    later = lax.ppermute(grad_filtered, CONTEXT, [(i + 1, i) for i in range(blocks - 1)])
    halo = filter_taps - 1
    gated_ext = jnp.concatenate([earlier[:, :, local_tokens - halo:], gated], 2)
    grad_ext = jnp.concatenate([grad_filtered, later[:, :, :halo]], 2)
    reversed_taps = long_filter[:, ::-1][:, None, :]
    tap_sums = lax.conv_general_dilated(
        gated_ext,
        grad_filtered,
        window_strides=(1,),
        padding=((0, 0),),
        dimension_numbers=lax.ConvDimensionNumbers((1, 0, 2), (1, 0, 2), (1, 0, 2)),
        batch_group_count=groups,
        preferred_element_type=jnp.float32,
    )
    partial_taps = tap_sums[:, 0, ::-1]
    rows = partial_taps.reshape(blocks, groups // blocks, filter_taps)
    forward = lambda lhs, rhs: grouped_conv(lhs, rhs, rhs.shape[0]).astype(jnp.bfloat16)
    rows = halving_step(rows, "core", 0)
    half = groups // 2
    rows, filtered_low = halving_step(
        rows, "y", 0, (forward, (gated_ext[:, :half], reversed_taps[:half]))
    )
    rows, filtered_high = halving_step(
        rows, "y", 1, (forward, (gated_ext[:, half:], reversed_taps[half:]))
    )
    filtered = jnp.concatenate([filtered_low, filtered_high], 1)
    rows, operands = lax.optimization_barrier((rows, (grad_ext, long_filter[:, None, :])))
    rows = lax.all_to_all(rows, "z", split_axis=0, concat_axis=0, tiled=True)
    rows, grad_gated = lax.optimization_barrier((rows, forward(*operands)))
    own_taps = jnp.sum(rows, axis=0, keepdims=True)
    filter_grads = butterfly_sum(own_taps[0], "tensor") * factor
    filtered_wide = filtered.astype(jnp.float32)
    grad_wide = grad_gated.astype(jnp.float32)
    mixed = (query_stream.astype(jnp.float32) * filtered_wide).astype(jnp.bfloat16)
    stream_grads = jnp.stack(
        [
            cotangent.astype(jnp.float32) * filtered_wide,
            grad_wide * value_stream.astype(jnp.float32),
            grad_wide * key_stream.astype(jnp.float32),
        ]
    ).astype(jnp.bfloat16)
    return (mixed, stream_grads, filter_grads)


def solution(mesh):
    contexts, tensors = mesh.devices.shape
    split = mesh.devices.reshape(contexts // 8, 4, 2, tensors)
    fine = jax.sharding.Mesh(split, CONTEXT + ("tensor",))
    in_specs = (P(None, "tensor", None, CONTEXT), P(), P("tensor", None, CONTEXT))
    out_specs = (
        P("tensor", None, CONTEXT),
        P(None, "tensor", None, CONTEXT),
        P(CONTEXT, None),
    )
    return jax.shard_map(body, mesh=fine, in_specs=in_specs, out_specs=out_specs, check_vma=False)
```
